512 devices in a mesh: snap: 8 (over y, x_lo), brick: 64 (over z, x_hi, core).
Axes of the slice: x: 4 (x_hi: 2, x_lo: 2; x = x_hi * 2 + x_lo), y: 4, z: 16, core: 2. Of those that a mesh axis runs over, the one named last changes fastest.
Arguments:
- positions: float32 [8, 3, 16384], P('snap', None, 'brick'), may hold values from 0 to 7, as said below
- species: int32 [8, 16384], P('snap', 'brick'), may hold values from 0 to 4
- atom_words: int32 [8, 16384], P('snap', 'brick'), may hold values from 0 to 32767, as said below
- left_vector: float32 [8, 3, 16384], P('snap', None, 'brick'), may hold values from -6 to 6
- right_vector: float32 [5, 81, 80], replicated, may hold values from -0.006 to 0.006
- direction: float32 [5, 81, 80], replicated, may hold values from -6 to 6
- solution: float32 [5, 81, 80], replicated, may hold values from -6 to 6
- scalars: float32 [3], replicated, may hold values from 0.0005 to 2, as said below
Outputs:
- left_next: float32 [8, 3, 16384], P('snap', None, 'brick')
- right_next: float32 [5, 81, 80], replicated
- direction_next: float32 [5, 81, 80], replicated
- solution_next: float32 [5, 81, 80], replicated
- scalars_next: float32 [3], replicated
The draws below stay inside these ranges and needn't reach their ends.
Inputs may be any that keep to these rules, and one draw needn't show every extreme that they name: `atom_words`: bit o-1 of atom g's word (o = 1..15) marks g+o as its neighbour; no bit points outside the snapshot. `positions`: rows 0 and 1 are transverse coordinates; row 2 is the offset along the column, below 0.2. `scalars`: alpha lies between 0.0005 and 0.002; rho_bar and phi_bar between 0.5 and 2.
All inputs are finite; a program needn't handle non-finite values.
Results may differ from the reference program's by a relative error of at most 0.0003.
Values sent between devices are 32-bit elements; how exact they have to be, the bound alone decides.
No kernel may reach another device: no remote copies, remote signals or barrier semaphores. Data moves between devices by JAX's collectives and lax.ppermute only.
A program may use at most 64 MiB of HBM per device.

```python
import math
import jax
import jax.numpy as jnp
from jax import lax

SPECIES = 5
RADIAL = 16
WINDOW = 15
ITERS = 3
CHANNELS = 80
SNAPS = 8
NATOMS = 16384


def draw_positions(key, part):
    plane_key, shift_key = jax.random.split(jax.random.fold_in(key, 11))
    atom_index = jnp.arange(NATOMS, dtype=jnp.float32)
    column_width = 3.5 + 3.5 * atom_index / NATOMS
    plane_coords = jax.random.uniform(plane_key, (SNAPS, 2, NATOMS), jnp.float32)
    shifts = 0.2 * jax.random.uniform(shift_key, (SNAPS, 1, NATOMS), jnp.float32)
    return jnp.concatenate([plane_coords * column_width[None, None, :], shifts], axis=1)


def draw_atom_words(key, part):
    upward = jax.random.randint(jax.random.fold_in(key, 23), (SNAPS, NATOMS), 0, 2 ** WINDOW, dtype=jnp.int32)
    atom_index = jnp.arange(NATOMS, dtype=jnp.int32)
    middle = NATOMS // 2
    full_run = (atom_index >= middle - WINDOW) & (atom_index <= middle)
    upward = jnp.where(full_run[None, :], 2 ** WINDOW - 1, upward)
    packed = jnp.zeros((SNAPS, NATOMS), jnp.int32)
    for offset in range(1, WINDOW + 1):
        inside = (atom_index + offset < NATOMS).astype(jnp.int32)
        upper_bit = jnp.bitwise_and(jnp.right_shift(upward, offset - 1), 1) * inside[None, :]
        packed = packed + upper_bit * 2 ** (offset - 1)
    return packed


def draw_scalars(key, part):
    first = jax.random.uniform(jax.random.fold_in(key, 31), (1,), jnp.float32, 0.0005, 0.002)
    rest = jax.random.uniform(jax.random.fold_in(key, 37), (2,), jnp.float32, 0.5, 2.0)
    return jnp.concatenate([first, rest])


def with_ends(drawn, key, smallest, top_value):
    longest = drawn.shape.index(max(drawn.shape))
    spots = []
    for shift in (0, 1):
        where = [jax.random.randint(jax.random.fold_in(key, axis), (), 0, length) for axis, length in enumerate(drawn.shape)]
        where[longest] = (where[longest] + shift) % drawn.shape[longest]
        spots.append(tuple(where))
    return drawn.at[spots[0]].set(smallest).at[spots[1]].set(top_value)


def level_of(rng, shape, cuts, least, top_value):
    gain = 1.0
    for dim, blocks in cuts:
        steps = jax.random.uniform(jax.random.fold_in(jax.random.fold_in(rng, 6), dim), (blocks,), jnp.float32, least / len(cuts), top_value / len(cuts))
        gain = gain * jnp.repeat(jnp.exp(steps), shape[dim] // blocks).reshape((-1,) + (1,) * (len(shape) - 1 - dim))
    return gain


def centred(own_key, dims, deviation, limit, cuts=(), kind=jnp.bfloat16):
    loudness = level_of(own_key, dims, cuts, -0.22, 0.18) if cuts else 1.0
    values = jax.random.normal(own_key, dims, jnp.float32) * deviation * loudness
    return jnp.minimum(jnp.maximum(values, -limit), limit).astype(kind)


def setup_inputs(seed: int = 0) -> dict:
    seeds = jax.random.split(jax.random.key(seed), 9)
    positions = draw_positions(jax.random.fold_in(seeds[8], 71), 0)
    species = with_ends(jax.random.randint(seeds[1], (SNAPS, NATOMS), 0, SPECIES), jax.random.fold_in(seeds[1], 1), 0, SPECIES - 1).astype(jnp.int32)
    atom_words = draw_atom_words(jax.random.fold_in(seeds[8], 71), 0)
    left_vector = centred(seeds[3], (SNAPS, 3, NATOMS), 1.0, 6.0, ((0, 8), (2, 64)), jnp.float32)
    right_vector = centred(seeds[4], (SPECIES, CHANNELS + 1, CHANNELS), 0.001, 0.006, (), jnp.float32)
    direction = centred(seeds[5], (SPECIES, CHANNELS + 1, CHANNELS), 1.0, 6.0, (), jnp.float32)
    solution = centred(seeds[6], (SPECIES, CHANNELS + 1, CHANNELS), 1.0, 6.0, (), jnp.float32)
    scalars = draw_scalars(jax.random.fold_in(seeds[8], 71), 0)
    return dict(positions=positions, species=species, atom_words=atom_words, left_vector=left_vector, right_vector=right_vector, direction=direction, solution=solution, scalars=scalars)


cutoff_sq = 36.0
spacing = 0.25
force_unit = 0.015625
tiny = 1e-06
HIGHEST = lax.Precision.HIGHEST

def window_offsets():
    return [shift_by for shift_by in range(1, WINDOW + 1)] + [-shift_by for shift_by in range(1, WINDOW + 1)]

def radial_tables(scaled):
    envelope = jnp.maximum(1.0 - scaled, 0.0)
    argument = 2.0 * jnp.minimum(scaled, 1.0) - 1.0
    first_kind = [jnp.ones_like(argument), argument]
    second_kind = [jnp.ones_like(argument), 2.0 * argument]
    for degree in range(2, RADIAL):
        first_kind.append(2.0 * argument * first_kind[-1] - first_kind[-2])
        second_kind.append(2.0 * argument * second_kind[-1] - second_kind[-2])
    values = []
    slopes = []
    for degree in range(RADIAL):
        damping = 1.0 / (1.0 + degree)
        values.append(envelope * envelope * first_kind[degree] * damping)
        derivative = -2.0 * envelope * first_kind[degree]
        if degree > 0:
            derivative = derivative + 2.0 * degree * envelope * envelope * second_kind[degree - 1]
        slopes.append(derivative * damping)
    return (jnp.stack(values, axis=1), jnp.stack(slopes, axis=1))

def shifted_stack(padded, atom_count):
    return jnp.stack([padded[:, WINDOW + offset:WINDOW + offset + atom_count] for offset in window_offsets()])

def pair_tables(padded, atom_count):
    offsets = window_offsets()
    here = padded[:, WINDOW:WINDOW + atom_count]
    there = shifted_stack(padded, atom_count)
    lift = jnp.array([0.0, 0.0, 1.0], jnp.float32)
    steps_z = jnp.array(offsets, jnp.float32) * spacing
    delta = there[:, :3, :] - here[None, :3, :] + steps_z[:, None, None] * lift[None, :, None]
    scaled = lax.optimization_barrier(jnp.sum(delta * delta, axis=1)) / cutoff_sq
    radial, slope = radial_tables(scaled)
    kinds = jnp.arange(SPECIES, dtype=jnp.float32)
    other = (there[:, 3:4, :] == kinds[None, :, None]).astype(jnp.float32)
    here_words = here[4].astype(jnp.int32)
    there_words = there[:, 4, :].astype(jnp.int32)
    upward = jnp.array([offset > 0 for offset in offsets])
    source = jnp.where(upward[:, None], here_words[None, :], there_words)
    bits = jnp.array([offset - 1 if offset > 0 else -offset - 1 for offset in offsets], jnp.int32)
    linked = jnp.bitwise_and(jnp.right_shift(source, bits[:, None]), 1).astype(jnp.float32)
    return (delta, radial, slope, other, linked)

def density(padded, atom_count):
    delta, radial, slope, other, linked = pair_tables(padded, atom_count)
    grid = jnp.einsum('ozi,oni->zni', other, radial * linked[:, None, :], precision=HIGHEST)
    return grid.reshape(SPECIES * RADIAL, atom_count)

def slope_field(field_density, own_kinds, coefs):
    channels = field_density.shape[0]
    result = jnp.zeros_like(field_density)
    for kind in range(SPECIES):
        quad = coefs[kind, :channels, :]
        part = coefs[kind, channels][:, None] + jnp.dot(quad + quad.T, field_density, precision=HIGHEST) / math.sqrt(channels)
        result = result + own_kinds[kind][None, :] * part
    return result

def pull_force(slopes, slopes_pad, padded, own_kinds, atom_count):
    delta, radial, slope, other, linked = pair_tables(padded, atom_count)
    own_grid = slopes.reshape(SPECIES, RADIAL, atom_count)
    there_slopes = shifted_stack(slopes_pad, atom_count).reshape(2 * WINDOW, SPECIES, RADIAL, atom_count)
    outward = jnp.einsum('ozi,zni->oni', other, own_grid, precision=HIGHEST)
    inward = jnp.einsum('zi,ozni->oni', own_kinds, there_slopes, precision=HIGHEST)
    strength = lax.optimization_barrier(jnp.sum((outward + inward) * slope, axis=1)) * linked * (2.0 / cutoff_sq)
    return lax.optimization_barrier(jnp.sum(strength[:, None, :] * delta, axis=0))

def back_local(field_density, values, value_pad, padded, own_kinds, atom_count):
    delta, radial, slope, other, linked = pair_tables(padded, atom_count)
    there_values = shifted_stack(value_pad, atom_count)
    project = lax.optimization_barrier(jnp.sum(delta * (values[None] - there_values), axis=1)) * linked * (2.0 / cutoff_sq)
    channels = field_density.shape[0]
    weights = jnp.einsum('ozi,oni->zni', other, slope * project[:, None, :], precision=HIGHEST).reshape(channels, atom_count)
    rows = []
    for kind in range(SPECIES):
        masked = field_density * own_kinds[kind][None, :]
        cross = jnp.dot(masked, weights.T, precision=HIGHEST)
        linear = lax.optimization_barrier(jnp.sum(weights * own_kinds[kind][None, :], axis=1))
        rows.append(jnp.concatenate([(cross + cross.T) / math.sqrt(channels), linear[None, :]], axis=0))
    return jnp.stack(rows)

def rotation(rho_bar, phi_bar, beta_norm, alpha_norm):
    rho_new = jnp.sqrt(rho_bar * rho_bar + beta_norm * beta_norm)
    cosine = rho_bar / rho_new
    sine_term = beta_norm / rho_new
    theta_term = sine_term * alpha_norm
    return (rho_new, theta_term, cosine * phi_bar, -cosine * alpha_norm, sine_term * phi_bar)

def reference(positions, species, atom_words, left_vector, right_vector, direction, solution, scalars):
    atom_count = NATOMS
    pad_edges = ((0, 0), (WINDOW, WINDOW))
    left_total = 3 * NATOMS * SNAPS
    coef_total = right_vector.size
    back_unit = force_unit * coef_total / left_total
    paddeds = []
    kinds_list = []
    densities = []
    for snapshot in range(SNAPS):
        geometry = jnp.concatenate([positions[snapshot], species[snapshot].astype(jnp.float32)[None], atom_words[snapshot].astype(jnp.float32)[None]], axis=0)
        padded = jnp.pad(geometry, pad_edges)
        own_kinds = (species[snapshot][None, :] == jnp.arange(SPECIES, dtype=jnp.int32)[:, None]).astype(jnp.float32)
        paddeds.append(padded)
        kinds_list.append(own_kinds)
        densities.append(density(padded, atom_count))
    alpha_norm = scalars[0]
    rho_bar = scalars[1]
    phi_bar = scalars[2]
    left_now = left_vector
    right_now = right_vector
    direction_now = direction
    solution_now = solution
    for sweep in range(ITERS):
        forces = []
        for snapshot in range(SNAPS):
            slopes = slope_field(densities[snapshot], kinds_list[snapshot], right_now)
            forces.append(pull_force(slopes, jnp.pad(slopes, pad_edges), paddeds[snapshot], kinds_list[snapshot], atom_count))
        left_now = force_unit * jnp.stack(forces) - alpha_norm * left_now
        beta_norm = jnp.sqrt(jnp.sum(left_now * left_now) / left_total + tiny)
        left_now = left_now / beta_norm
        totals = jnp.zeros_like(right_now)
        for snapshot in range(SNAPS):
            totals = totals + back_local(densities[snapshot], left_now[snapshot], jnp.pad(left_now[snapshot], pad_edges), paddeds[snapshot], kinds_list[snapshot], atom_count)
        right_now = back_unit * totals - beta_norm * right_now
        alpha_norm = jnp.sqrt(jnp.sum(right_now * right_now) / coef_total + tiny)
        right_now = right_now / alpha_norm
        rho_new, theta_term, phi_term, rho_bar, phi_bar = rotation(rho_bar, phi_bar, beta_norm, alpha_norm)
        solution_now = solution_now + phi_term / rho_new * direction_now
        direction_now = right_now - theta_term / rho_new * direction_now
    return (left_now, right_now, direction_now, solution_now, jnp.stack([alpha_norm, rho_bar, phi_bar]))
```

```python
import functools
import math

import jax
import jax.numpy as jnp
from jax import lax
from jax.sharding import Mesh
from jax.sharding import PartitionSpec as P

SPECIES = 5
RADIAL = 16
WINDOW = 15
ITERS = 3
SNAP = ("snap_0", "snap_1")
BRICK = ("brick_0", "brick_1", "brick_2")
SNAP_BRICK = ("snap_0", "snap_1", "brick_0", "brick_1", "brick_2")


cutoff_sq = 36.0
spacing = 0.25
force_unit = 0.015625
tiny = 1e-06
HIGHEST = lax.Precision.HIGHEST


def with_halo(cells, sides, width):
    for axis, dim in sides:
        count = lax.axis_size(axis)
        ends = count - 1
        head = lax.slice_in_dim(cells, 0, width, axis=dim)
        tail = lax.slice_in_dim(cells, cells.shape[dim] - width, cells.shape[dim], axis=dim)
        cells = jnp.concatenate(
            [
                lax.ppermute(tail, axis, [(i, (i + 1) % count) for i in range(ends)]),
                cells,
                lax.ppermute(head, axis, [((i + 1) % count, i) for i in range(ends)]),
            ],
            axis=dim,
        )
    return cells


def by_axis(shard, axes):
    return functools.reduce(lax.psum, axes, shard)


def window_offsets():
    return [shift_by for shift_by in range(1, WINDOW + 1)] + [
        -shift_by for shift_by in range(1, WINDOW + 1)
    ]


def radial_tables(scaled):
    envelope = jnp.maximum(1.0 - scaled, 0.0)
    argument = 2.0 * jnp.minimum(scaled, 1.0) - 1.0
    first_kind = [jnp.ones_like(argument), argument]
    second_kind = [jnp.ones_like(argument), 2.0 * argument]
    for degree in range(2, RADIAL):
        first_kind.append(2.0 * argument * first_kind[-1] - first_kind[-2])
        second_kind.append(2.0 * argument * second_kind[-1] - second_kind[-2])
    values = []
    slopes = []
    for degree in range(RADIAL):
        damping = 1.0 / (1.0 + degree)
        values.append(envelope * envelope * first_kind[degree] * damping)
        derivative = -2.0 * envelope * first_kind[degree]
        if degree > 0:
            derivative = derivative + 2.0 * degree * envelope * envelope * second_kind[degree - 1]
        slopes.append(derivative * damping)
    return (jnp.stack(values, axis=1), jnp.stack(slopes, axis=1))


def shifted_stack(padded, atom_count):
    return jnp.stack(
        [padded[:, WINDOW + offset : WINDOW + offset + atom_count] for offset in window_offsets()]
    )


def pair_tables(padded, atom_count):
    offsets = window_offsets()
    here = padded[:, WINDOW : WINDOW + atom_count]
    there = shifted_stack(padded, atom_count)
    lift = jnp.array([0.0, 0.0, 1.0], jnp.float32)
    steps_z = jnp.array(offsets, jnp.float32) * spacing
    delta = there[:, :3, :] - here[None, :3, :] + steps_z[:, None, None] * lift[None, :, None]
    scaled = jnp.sum(delta * delta, axis=1) / cutoff_sq
    radial, slope = radial_tables(scaled)
    kinds = jnp.arange(SPECIES, dtype=jnp.float32)
    other = (there[:, 3:4, :] == kinds[None, :, None]).astype(jnp.float32)
    here_words = here[4].astype(jnp.int32)
    there_words = there[:, 4, :].astype(jnp.int32)
    upward = jnp.array([offset > 0 for offset in offsets])
    source = jnp.where(upward[:, None], here_words[None, :], there_words)
    bits = jnp.array([offset - 1 if offset > 0 else -offset - 1 for offset in offsets], jnp.int32)
    linked = jnp.bitwise_and(jnp.right_shift(source, bits[:, None]), 1).astype(jnp.float32)
    return (delta, radial, slope, other, linked)


def density(padded, atom_count):
    delta, radial, slope, other, linked = pair_tables(padded, atom_count)
    grid = jnp.einsum("ozi,oni->zni", other, radial * linked[:, None, :], precision=HIGHEST)
    return grid.reshape(SPECIES * RADIAL, atom_count)


def slope_field(field_density, own_kinds, coefs):
    channels = field_density.shape[0]
    result = jnp.zeros_like(field_density)
    for kind in range(SPECIES):
        quad = coefs[kind, :channels, :]
        part = coefs[kind, channels][:, None] + jnp.dot(
            quad + quad.T, field_density, precision=HIGHEST
        ) / math.sqrt(channels)
        result = result + own_kinds[kind][None, :] * part
    return result


def pull_force(slopes, slopes_pad, padded, own_kinds, atom_count):
    delta, radial, slope, other, linked = pair_tables(padded, atom_count)
    own_grid = slopes.reshape(SPECIES, RADIAL, atom_count)
    there_slopes = shifted_stack(slopes_pad, atom_count).reshape(
        2 * WINDOW, SPECIES, RADIAL, atom_count
    )
    outward = jnp.einsum("ozi,zni->oni", other, own_grid, precision=HIGHEST)
    inward = jnp.einsum("zi,ozni->oni", own_kinds, there_slopes, precision=HIGHEST)
    strength = jnp.sum((outward + inward) * slope, axis=1) * linked * (2.0 / cutoff_sq)
    return jnp.sum(strength[:, None, :] * delta, axis=0)


def back_terms(field_density, values, value_pad, padded, own_kinds, atom_count):
    delta, radial, slope, other, linked = pair_tables(padded, atom_count)
    there_values = shifted_stack(value_pad, atom_count)
    project = jnp.sum(delta * (values[None] - there_values), axis=1) * linked * (2.0 / cutoff_sq)
    channels = field_density.shape[0]
    weights = jnp.einsum(
        "ozi,oni->zni", other, slope * project[:, None, :], precision=HIGHEST
    ).reshape(channels, atom_count)
    rows = []
    for kind in range(SPECIES):
        masked = field_density * own_kinds[kind][None, :]
        cross = jnp.dot(masked, weights.T, precision=HIGHEST)
        linear = jnp.sum(weights * own_kinds[kind][None, :], axis=1)
        rows.append(
            jnp.concatenate([(cross + cross.T) / math.sqrt(channels), linear[None, :]], axis=0)
        )
    return jnp.stack(rows)


def rotation(rho_bar, phi_bar, beta_norm, alpha_norm):
    rho_new = jnp.sqrt(rho_bar * rho_bar + beta_norm * beta_norm)
    cosine = rho_bar / rho_new
    sine_term = beta_norm / rho_new
    theta_term = sine_term * alpha_norm
    return (rho_new, theta_term, cosine * phi_bar, -cosine * alpha_norm, sine_term * phi_bar)


def shards(positions, species, atom_words, left_vector, right_vector, direction, solution, scalars):
    atom_count = positions.shape[2]
    coef_total = right_vector.size
    devices_all = lax.axis_size(SNAP) * lax.axis_size(BRICK)
    left_total = 3 * atom_count * positions.shape[0] * devices_all
    back_unit = force_unit * coef_total / left_total
    geometry = jnp.concatenate(
        [
            positions[0],
            species[0].astype(jnp.float32)[None],
            atom_words[0].astype(jnp.float32)[None],
        ],
        axis=0,
    )
    depth = 3 * WINDOW
    padded_all = with_halo(geometry, ((BRICK, 1),), depth)
    kind_values = jnp.arange(SPECIES, dtype=jnp.float32)
    ext_count = atom_count + 4 * WINDOW
    mid_count = atom_count + 2 * WINDOW
    density_ext = density(padded_all, ext_count)
    kinds_ext = (
        padded_all[3, WINDOW : WINDOW + ext_count][None, :] == kind_values[:, None]
    ).astype(jnp.float32)
    field_density = density_ext[:, 2 * WINDOW : 2 * WINDOW + atom_count]
    own_kinds = kinds_ext[:, 2 * WINDOW : 2 * WINDOW + atom_count]
    padded = padded_all[:, 2 * WINDOW : 4 * WINDOW + atom_count]
    mid_geometry = padded_all[:, WINDOW : 3 * WINDOW + mid_count]
    mid_kinds = kinds_ext[:, WINDOW : WINDOW + mid_count]
    left_ext = with_halo(left_vector[0], ((BRICK, 1),), WINDOW)
    alpha_norm = scalars[0]
    rho_bar = scalars[1]
    phi_bar = scalars[2]
    left_now = left_vector[0]
    right_now = right_vector
    direction_now = direction
    solution_now = solution
    for sweep in range(ITERS):
        slopes_ext = slope_field(density_ext, kinds_ext, right_now)
        force_ext = pull_force(
            slopes_ext[:, WINDOW : WINDOW + mid_count],
            slopes_ext,
            mid_geometry,
            mid_kinds,
            mid_count,
        )
        raw_pad = force_unit * force_ext - alpha_norm * left_ext
        raw_left = raw_pad[:, WINDOW : WINDOW + atom_count]
        local_terms = back_terms(field_density, raw_left, raw_pad, padded, own_kinds, atom_count)
        packed = jnp.concatenate(
            [local_terms.reshape(-1), jnp.sum(raw_left * raw_left)[None]]
        )
        packed = lax.psum(packed, SNAP_BRICK)
        totals = packed[:-1].reshape(local_terms.shape)
        squares = packed[-1]
        beta_norm = jnp.sqrt(squares / left_total + tiny)
        left_now = raw_left / beta_norm
        right_raw = back_unit * totals / beta_norm - beta_norm * right_now
        left_ext = raw_pad / beta_norm
        alpha_norm = jnp.sqrt(jnp.sum(right_raw * right_raw) / coef_total + tiny)
        right_now = right_raw / alpha_norm
        rho_new, theta_term, phi_term, rho_bar, phi_bar = rotation(
            rho_bar, phi_bar, beta_norm, alpha_norm
        )
        solution_now = solution_now + phi_term / rho_new * direction_now
        direction_now = right_now - theta_term / rho_new * direction_now
    scalars_next = jnp.stack([alpha_norm, rho_bar, phi_bar])
    return (left_now[None], right_now, direction_now, solution_now, scalars_next)


def solution(mesh):
    torus = Mesh(
        mesh.devices.reshape(4, 2, 16, 2, 2), ("snap_0", "snap_1", "brick_0", "brick_1", "brick_2")
    )
    return jax.shard_map(
        shards,
        mesh=torus,
        in_specs=(
            P(SNAP, None, BRICK),
            P(SNAP, BRICK),
            P(SNAP, BRICK),
            P(SNAP, None, BRICK),
            P(),
            P(),
            P(),
            P(),
        ),
        out_specs=(P(SNAP, None, BRICK), P(), P(), P(), P()),
        check_vma=False,
    )
```

```python
import functools
import math

import jax
import jax.numpy as jnp
from jax import lax
from jax.sharding import Mesh
from jax.sharding import PartitionSpec as P

SPECIES = 5
RADIAL = 16
WINDOW = 15
ITERS = 3
SNAP = ("snap_0", "snap_1")
BRICK = ("brick_0", "brick_1", "brick_2")
SNAP_BRICK = ("snap_0", "snap_1", "brick_0", "brick_1", "brick_2")
BUTTERFLY_ORDER = ("brick_2", "snap_1", "brick_1", "snap_0", "brick_0")


cutoff_sq = 36.0
spacing = 0.25
force_unit = 0.015625
tiny = 1e-06
HIGHEST = lax.Precision.HIGHEST


def with_halo(cells, sides, width):
    for axis, dim in sides:
        count = lax.axis_size(axis)
        ends = count - 1
        head = lax.slice_in_dim(cells, 0, width, axis=dim)
        tail = lax.slice_in_dim(cells, cells.shape[dim] - width, cells.shape[dim], axis=dim)
        cells = jnp.concatenate(
            [
                lax.ppermute(tail, axis, [(i, (i + 1) % count) for i in range(ends)]),
                cells,
                lax.ppermute(head, axis, [((i + 1) % count, i) for i in range(ends)]),
            ],
            axis=dim,
        )
    return cells


def by_axis(shard, axes):
    return functools.reduce(lax.psum, axes, shard)


def butterfly_sum(shard, axes):
    for axis in axes:
        count = lax.axis_size(axis)
        step = 1
        while step < count:
            partners = [(i, i ^ step) for i in range(count)]
            shard = shard + lax.ppermute(shard, axis, partners)
            step *= 2
    return shard


def window_offsets():
    return [shift_by for shift_by in range(1, WINDOW + 1)] + [
        -shift_by for shift_by in range(1, WINDOW + 1)
    ]


def radial_tables(scaled):
    envelope = jnp.maximum(1.0 - scaled, 0.0)
    argument = 2.0 * jnp.minimum(scaled, 1.0) - 1.0
    first_kind = [jnp.ones_like(argument), argument]
    second_kind = [jnp.ones_like(argument), 2.0 * argument]
    for degree in range(2, RADIAL):
        first_kind.append(2.0 * argument * first_kind[-1] - first_kind[-2])
        second_kind.append(2.0 * argument * second_kind[-1] - second_kind[-2])
    values = []
    slopes = []
    for degree in range(RADIAL):
        damping = 1.0 / (1.0 + degree)
        values.append(envelope * envelope * first_kind[degree] * damping)
        derivative = -2.0 * envelope * first_kind[degree]
        if degree > 0:
            derivative = derivative + 2.0 * degree * envelope * envelope * second_kind[degree - 1]
        slopes.append(derivative * damping)
    return (jnp.stack(values, axis=1), jnp.stack(slopes, axis=1))


def shifted_stack(padded, atom_count):
    return jnp.stack(
        [padded[:, WINDOW + offset : WINDOW + offset + atom_count] for offset in window_offsets()]
    )


def pair_tables(padded, atom_count):
    offsets = window_offsets()
    here = padded[:, WINDOW : WINDOW + atom_count]
    there = shifted_stack(padded, atom_count)
    lift = jnp.array([0.0, 0.0, 1.0], jnp.float32)
    steps_z = jnp.array(offsets, jnp.float32) * spacing
    delta = there[:, :3, :] - here[None, :3, :] + steps_z[:, None, None] * lift[None, :, None]
    scaled = jnp.sum(delta * delta, axis=1) / cutoff_sq
    radial, slope = radial_tables(scaled)
    kinds = jnp.arange(SPECIES, dtype=jnp.float32)
    other = (there[:, 3:4, :] == kinds[None, :, None]).astype(jnp.float32)
    here_words = here[4].astype(jnp.int32)
    there_words = there[:, 4, :].astype(jnp.int32)
    upward = jnp.array([offset > 0 for offset in offsets])
    source = jnp.where(upward[:, None], here_words[None, :], there_words)
    bits = jnp.array([offset - 1 if offset > 0 else -offset - 1 for offset in offsets], jnp.int32)
    linked = jnp.bitwise_and(jnp.right_shift(source, bits[:, None]), 1).astype(jnp.float32)
    return (delta, radial, slope, other, linked)


def density(padded, atom_count):
    delta, radial, slope, other, linked = pair_tables(padded, atom_count)
    grid = jnp.einsum("ozi,oni->zni", other, radial * linked[:, None, :], precision=HIGHEST)
    return grid.reshape(SPECIES * RADIAL, atom_count)


def slope_field(field_density, own_kinds, coefs):
    channels = field_density.shape[0]
    result = jnp.zeros_like(field_density)
    for kind in range(SPECIES):
        quad = coefs[kind, :channels, :]
        part = coefs[kind, channels][:, None] + jnp.dot(
            quad + quad.T, field_density, precision=HIGHEST
        ) / math.sqrt(channels)
        result = result + own_kinds[kind][None, :] * part
    return result


def pull_force(slopes, slopes_pad, padded, own_kinds, atom_count):
    delta, radial, slope, other, linked = pair_tables(padded, atom_count)
    own_grid = slopes.reshape(SPECIES, RADIAL, atom_count)
    there_slopes = shifted_stack(slopes_pad, atom_count).reshape(
        2 * WINDOW, SPECIES, RADIAL, atom_count
    )
    outward = jnp.einsum("ozi,zni->oni", other, own_grid, precision=HIGHEST)
    inward = jnp.einsum("zi,ozni->oni", own_kinds, there_slopes, precision=HIGHEST)
    strength = jnp.sum((outward + inward) * slope, axis=1) * linked * (2.0 / cutoff_sq)
    return jnp.sum(strength[:, None, :] * delta, axis=0)


def back_terms(field_density, values, value_pad, padded, own_kinds, atom_count):
    delta, radial, slope, other, linked = pair_tables(padded, atom_count)
    there_values = shifted_stack(value_pad, atom_count)
    project = jnp.sum(delta * (values[None] - there_values), axis=1) * linked * (2.0 / cutoff_sq)
    channels = field_density.shape[0]
    weights = jnp.einsum(
        "ozi,oni->zni", other, slope * project[:, None, :], precision=HIGHEST
    ).reshape(channels, atom_count)
    rows = []
    for kind in range(SPECIES):
        masked = field_density * own_kinds[kind][None, :]
        cross = jnp.dot(masked, weights.T, precision=HIGHEST)
        linear = jnp.sum(weights * own_kinds[kind][None, :], axis=1)
        rows.append(
            jnp.concatenate([(cross + cross.T) / math.sqrt(channels), linear[None, :]], axis=0)
        )
    return jnp.stack(rows)


def rotation(rho_bar, phi_bar, beta_norm, alpha_norm):
    rho_new = jnp.sqrt(rho_bar * rho_bar + beta_norm * beta_norm)
    cosine = rho_bar / rho_new
    sine_term = beta_norm / rho_new
    theta_term = sine_term * alpha_norm
    return (rho_new, theta_term, cosine * phi_bar, -cosine * alpha_norm, sine_term * phi_bar)


def shards(positions, species, atom_words, left_vector, right_vector, direction, solution, scalars):
    atom_count = positions.shape[2]
    coef_total = right_vector.size
    devices_all = lax.axis_size(SNAP) * lax.axis_size(BRICK)
    left_total = 3 * atom_count * positions.shape[0] * devices_all
    back_unit = force_unit * coef_total / left_total
    geometry = jnp.concatenate(
        [
            positions[0],
            species[0].astype(jnp.float32)[None],
            atom_words[0].astype(jnp.float32)[None],
        ],
        axis=0,
    )
    depth = 3 * WINDOW
    padded_all = with_halo(geometry, ((BRICK, 1),), depth)
    kind_values = jnp.arange(SPECIES, dtype=jnp.float32)
    ext_count = atom_count + 4 * WINDOW
    mid_count = atom_count + 2 * WINDOW
    density_ext = density(padded_all, ext_count)
    kinds_ext = (
        padded_all[3, WINDOW : WINDOW + ext_count][None, :] == kind_values[:, None]
    ).astype(jnp.float32)
    field_density = density_ext[:, 2 * WINDOW : 2 * WINDOW + atom_count]
    own_kinds = kinds_ext[:, 2 * WINDOW : 2 * WINDOW + atom_count]
    padded = padded_all[:, 2 * WINDOW : 4 * WINDOW + atom_count]
    mid_geometry = padded_all[:, WINDOW : 3 * WINDOW + mid_count]
    mid_kinds = kinds_ext[:, WINDOW : WINDOW + mid_count]
    left_ext = with_halo(left_vector[0], ((BRICK, 1),), WINDOW)
    alpha_norm = scalars[0]
    rho_bar = scalars[1]
    phi_bar = scalars[2]
    left_now = left_vector[0]
    right_now = right_vector
    direction_now = direction
    solution_now = solution
    for sweep in range(ITERS):
        slopes_ext = slope_field(density_ext, kinds_ext, right_now)
        force_ext = pull_force(
            slopes_ext[:, WINDOW : WINDOW + mid_count],
            slopes_ext,
            mid_geometry,
            mid_kinds,
            mid_count,
        )
        raw_pad = force_unit * force_ext - alpha_norm * left_ext
        raw_left = raw_pad[:, WINDOW : WINDOW + atom_count]
        local_terms = back_terms(field_density, raw_left, raw_pad, padded, own_kinds, atom_count)
        packed = jnp.concatenate(
            [local_terms.reshape(-1), jnp.sum(raw_left * raw_left)[None]]
        )
        packed = butterfly_sum(packed, BUTTERFLY_ORDER)
        totals = packed[:-1].reshape(local_terms.shape)
        squares = packed[-1]
        beta_norm = jnp.sqrt(squares / left_total + tiny)
        left_now = raw_left / beta_norm
        right_raw = back_unit * totals / beta_norm - beta_norm * right_now
        left_ext = raw_pad / beta_norm
        alpha_norm = jnp.sqrt(jnp.sum(right_raw * right_raw) / coef_total + tiny)
        right_now = right_raw / alpha_norm
        rho_new, theta_term, phi_term, rho_bar, phi_bar = rotation(
            rho_bar, phi_bar, beta_norm, alpha_norm
        )
        solution_now = solution_now + phi_term / rho_new * direction_now
        direction_now = right_now - theta_term / rho_new * direction_now
    scalars_next = jnp.stack([alpha_norm, rho_bar, phi_bar])
    return (left_now[None], right_now, direction_now, solution_now, scalars_next)


def solution(mesh):
    torus = Mesh(
        mesh.devices.reshape(4, 2, 16, 2, 2), ("snap_0", "snap_1", "brick_0", "brick_1", "brick_2")
    )
    return jax.shard_map(
        shards,
        mesh=torus,
        in_specs=(
            P(SNAP, None, BRICK),
            P(SNAP, BRICK),
            P(SNAP, BRICK),
            P(SNAP, None, BRICK),
            P(),
            P(),
            P(),
            P(),
        ),
        out_specs=(P(SNAP, None, BRICK), P(), P(), P(), P()),
        check_vma=False,
    )
```

```python
import functools
import math

import jax
import jax.numpy as jnp
from jax import lax
from jax.sharding import Mesh
from jax.sharding import PartitionSpec as P

SPECIES = 5
RADIAL = 16
WINDOW = 15
ITERS = 3
SNAP = ("snap_0", "snap_1")
BRICK = ("brick_0", "brick_1", "brick_2")
SNAP_BRICK = ("snap_0", "snap_1", "brick_0", "brick_1", "brick_2")
BUTTERFLY_ORDER = ("brick_2", "snap_1", "brick_1", "snap_0")


cutoff_sq = 36.0
spacing = 0.25
force_unit = 0.015625
tiny = 1e-06
HIGHEST = lax.Precision.HIGHEST


def with_halo(cells, sides, width):
    for axis, dim in sides:
        count = lax.axis_size(axis)
        ends = count - 1
        head = lax.slice_in_dim(cells, 0, width, axis=dim)
        tail = lax.slice_in_dim(cells, cells.shape[dim] - width, cells.shape[dim], axis=dim)
        cells = jnp.concatenate(
            [
                lax.ppermute(tail, axis, [(i, (i + 1) % count) for i in range(ends)]),
                cells,
                lax.ppermute(head, axis, [((i + 1) % count, i) for i in range(ends)]),
            ],
            axis=dim,
        )
    return cells


def by_axis(shard, axes):
    return functools.reduce(lax.psum, axes, shard)


def group_sum(shard, spread_axis, axes):
    count = lax.axis_size(spread_axis)
    length = shard.shape[0]
    padded = jnp.pad(shard, (0, (-length) % count))
    parts = lax.all_to_all(padded.reshape(count, -1), spread_axis, 0, 0, tiled=False)
    mine = butterfly_sum(jnp.sum(parts, axis=0), axes)
    spread = jnp.broadcast_to(mine[None], (count,) + mine.shape)
    whole = lax.all_to_all(spread, spread_axis, 0, 0, tiled=False)
    return whole.reshape(-1)[:length]


def butterfly_sum(shard, axes):
    for axis in axes:
        count = lax.axis_size(axis)
        step = 1
        while step < count:
            partners = [(i, i ^ step) for i in range(count)]
            shard = shard + lax.ppermute(shard, axis, partners)
            step *= 2
    return shard


def window_offsets():
    return [shift_by for shift_by in range(1, WINDOW + 1)] + [
        -shift_by for shift_by in range(1, WINDOW + 1)
    ]


def radial_tables(scaled):
    envelope = jnp.maximum(1.0 - scaled, 0.0)
    argument = 2.0 * jnp.minimum(scaled, 1.0) - 1.0
    first_kind = [jnp.ones_like(argument), argument]
    second_kind = [jnp.ones_like(argument), 2.0 * argument]
    for degree in range(2, RADIAL):
        first_kind.append(2.0 * argument * first_kind[-1] - first_kind[-2])
        second_kind.append(2.0 * argument * second_kind[-1] - second_kind[-2])
    values = []
    slopes = []
    for degree in range(RADIAL):
        damping = 1.0 / (1.0 + degree)
        values.append(envelope * envelope * first_kind[degree] * damping)
        derivative = -2.0 * envelope * first_kind[degree]
        if degree > 0:
            derivative = derivative + 2.0 * degree * envelope * envelope * second_kind[degree - 1]
        slopes.append(derivative * damping)
    return (jnp.stack(values, axis=1), jnp.stack(slopes, axis=1))


def shifted_stack(padded, atom_count):
    return jnp.stack(
        [padded[:, WINDOW + offset : WINDOW + offset + atom_count] for offset in window_offsets()]
    )


def pair_tables(padded, atom_count):
    offsets = window_offsets()
    here = padded[:, WINDOW : WINDOW + atom_count]
    there = shifted_stack(padded, atom_count)
    lift = jnp.array([0.0, 0.0, 1.0], jnp.float32)
    steps_z = jnp.array(offsets, jnp.float32) * spacing
    delta = there[:, :3, :] - here[None, :3, :] + steps_z[:, None, None] * lift[None, :, None]
    scaled = jnp.sum(delta * delta, axis=1) / cutoff_sq
    radial, slope = radial_tables(scaled)
    kinds = jnp.arange(SPECIES, dtype=jnp.float32)
    other = (there[:, 3:4, :] == kinds[None, :, None]).astype(jnp.float32)
    here_words = here[4].astype(jnp.int32)
    there_words = there[:, 4, :].astype(jnp.int32)
    upward = jnp.array([offset > 0 for offset in offsets])
    source = jnp.where(upward[:, None], here_words[None, :], there_words)
    bits = jnp.array([offset - 1 if offset > 0 else -offset - 1 for offset in offsets], jnp.int32)
    linked = jnp.bitwise_and(jnp.right_shift(source, bits[:, None]), 1).astype(jnp.float32)
    return (delta, radial, slope, other, linked)


def density(padded, atom_count):
    delta, radial, slope, other, linked = pair_tables(padded, atom_count)
    grid = jnp.einsum("ozi,oni->zni", other, radial * linked[:, None, :], precision=HIGHEST)
    return grid.reshape(SPECIES * RADIAL, atom_count)


def slope_field(field_density, own_kinds, coefs):
    channels = field_density.shape[0]
    result = jnp.zeros_like(field_density)
    for kind in range(SPECIES):
        quad = coefs[kind, :channels, :]
        part = coefs[kind, channels][:, None] + jnp.dot(
            quad + quad.T, field_density, precision=HIGHEST
        ) / math.sqrt(channels)
        result = result + own_kinds[kind][None, :] * part
    return result


def pull_force(slopes, slopes_pad, padded, own_kinds, atom_count):
    delta, radial, slope, other, linked = pair_tables(padded, atom_count)
    own_grid = slopes.reshape(SPECIES, RADIAL, atom_count)
    there_slopes = shifted_stack(slopes_pad, atom_count).reshape(
        2 * WINDOW, SPECIES, RADIAL, atom_count
    )
    outward = jnp.einsum("ozi,zni->oni", other, own_grid, precision=HIGHEST)
    inward = jnp.einsum("zi,ozni->oni", own_kinds, there_slopes, precision=HIGHEST)
    strength = jnp.sum((outward + inward) * slope, axis=1) * linked * (2.0 / cutoff_sq)
    return jnp.sum(strength[:, None, :] * delta, axis=0)


def back_terms(field_density, values, value_pad, padded, own_kinds, atom_count):
    delta, radial, slope, other, linked = pair_tables(padded, atom_count)
    there_values = shifted_stack(value_pad, atom_count)
    project = jnp.sum(delta * (values[None] - there_values), axis=1) * linked * (2.0 / cutoff_sq)
    channels = field_density.shape[0]
    weights = jnp.einsum(
        "ozi,oni->zni", other, slope * project[:, None, :], precision=HIGHEST
    ).reshape(channels, atom_count)
    rows = []
    for kind in range(SPECIES):
        masked = field_density * own_kinds[kind][None, :]
        cross = jnp.dot(masked, weights.T, precision=HIGHEST)
        linear = jnp.sum(weights * own_kinds[kind][None, :], axis=1)
        rows.append(
            jnp.concatenate([(cross + cross.T) / math.sqrt(channels), linear[None, :]], axis=0)
        )
    return jnp.stack(rows)


def rotation(rho_bar, phi_bar, beta_norm, alpha_norm):
    rho_new = jnp.sqrt(rho_bar * rho_bar + beta_norm * beta_norm)
    cosine = rho_bar / rho_new
    sine_term = beta_norm / rho_new
    theta_term = sine_term * alpha_norm
    return (rho_new, theta_term, cosine * phi_bar, -cosine * alpha_norm, sine_term * phi_bar)


def shards(positions, species, atom_words, left_vector, right_vector, direction, solution, scalars):
    atom_count = positions.shape[2]
    coef_total = right_vector.size
    devices_all = lax.axis_size(SNAP) * lax.axis_size(BRICK)
    left_total = 3 * atom_count * positions.shape[0] * devices_all
    back_unit = force_unit * coef_total / left_total
    geometry = jnp.concatenate(
        [
            positions[0],
            species[0].astype(jnp.float32)[None],
            atom_words[0].astype(jnp.float32)[None],
        ],
        axis=0,
    )
    depth = 3 * WINDOW
    padded_all = with_halo(geometry, ((BRICK, 1),), depth)
    kind_values = jnp.arange(SPECIES, dtype=jnp.float32)
    ext_count = atom_count + 4 * WINDOW
    mid_count = atom_count + 2 * WINDOW
    density_ext = density(padded_all, ext_count)
    kinds_ext = (
        padded_all[3, WINDOW : WINDOW + ext_count][None, :] == kind_values[:, None]
    ).astype(jnp.float32)
    field_density = density_ext[:, 2 * WINDOW : 2 * WINDOW + atom_count]
    own_kinds = kinds_ext[:, 2 * WINDOW : 2 * WINDOW + atom_count]
    padded = padded_all[:, 2 * WINDOW : 4 * WINDOW + atom_count]
    mid_geometry = padded_all[:, WINDOW : 3 * WINDOW + mid_count]
    mid_kinds = kinds_ext[:, WINDOW : WINDOW + mid_count]
    left_ext = with_halo(left_vector[0], ((BRICK, 1),), WINDOW)
    alpha_norm = scalars[0]
    rho_bar = scalars[1]
    phi_bar = scalars[2]
    left_now = left_vector[0]
    right_now = right_vector
    direction_now = direction
    solution_now = solution
    for sweep in range(ITERS):
        slopes_ext = slope_field(density_ext, kinds_ext, right_now)
        force_ext = pull_force(
            slopes_ext[:, WINDOW : WINDOW + mid_count],
            slopes_ext,
            mid_geometry,
            mid_kinds,
            mid_count,
        )
        raw_pad = force_unit * force_ext - alpha_norm * left_ext
        raw_left = raw_pad[:, WINDOW : WINDOW + atom_count]
        local_terms = back_terms(field_density, raw_left, raw_pad, padded, own_kinds, atom_count)
        packed = jnp.concatenate(
            [local_terms.reshape(-1), jnp.sum(raw_left * raw_left)[None]]
        )
        packed = group_sum(packed, "brick_0", BUTTERFLY_ORDER)
        totals = packed[:-1].reshape(local_terms.shape)
        squares = packed[-1]
        beta_norm = jnp.sqrt(squares / left_total + tiny)
        left_now = raw_left / beta_norm
        right_raw = back_unit * totals / beta_norm - beta_norm * right_now
        left_ext = raw_pad / beta_norm
        alpha_norm = jnp.sqrt(jnp.sum(right_raw * right_raw) / coef_total + tiny)
        right_now = right_raw / alpha_norm
        rho_new, theta_term, phi_term, rho_bar, phi_bar = rotation(
            rho_bar, phi_bar, beta_norm, alpha_norm
        )
        solution_now = solution_now + phi_term / rho_new * direction_now
        direction_now = right_now - theta_term / rho_new * direction_now
    scalars_next = jnp.stack([alpha_norm, rho_bar, phi_bar])
    return (left_now[None], right_now, direction_now, solution_now, scalars_next)


def solution(mesh):
    torus = Mesh(
        mesh.devices.reshape(4, 2, 16, 2, 2), ("snap_0", "snap_1", "brick_0", "brick_1", "brick_2")
    )
    return jax.shard_map(
        shards,
        mesh=torus,
        in_specs=(
            P(SNAP, None, BRICK),
            P(SNAP, BRICK),
            P(SNAP, BRICK),
            P(SNAP, None, BRICK),
            P(),
            P(),
            P(),
            P(),
        ),
        out_specs=(P(SNAP, None, BRICK), P(), P(), P(), P()),
        check_vma=False,
    )
```

```python
import functools
import math

import jax
import jax.numpy as jnp
from jax import lax
from jax.sharding import Mesh
from jax.sharding import PartitionSpec as P

SPECIES = 5
RADIAL = 16
WINDOW = 15
ITERS = 3
SNAP = ("snap_0", "snap_1")
BRICK = ("brick_0", "brick_1", "brick_2")
SNAP_BRICK = ("snap_0", "snap_1", "brick_0", "brick_1", "brick_2")
BUTTERFLY_ORDER = ("brick_2", "snap_1", "brick_1", "snap_0")


cutoff_sq = 36.0
spacing = 0.25
force_unit = 0.015625
tiny = 1e-06
HIGHEST = lax.Precision.HIGHEST


def with_halo(cells, sides, width):
    for axis, dim in sides:
        count = lax.axis_size(axis)
        ends = count - 1
        head = lax.slice_in_dim(cells, 0, width, axis=dim)
        tail = lax.slice_in_dim(cells, cells.shape[dim] - width, cells.shape[dim], axis=dim)
        cells = jnp.concatenate(
            [
                lax.ppermute(tail, axis, [(i, (i + 1) % count) for i in range(ends)]),
                cells,
                lax.ppermute(head, axis, [((i + 1) % count, i) for i in range(ends)]),
            ],
            axis=dim,
        )
    return cells


def by_axis(shard, axes):
    return functools.reduce(lax.psum, axes, shard)


def group_sum(shard, spread_axis, axes):
    count = lax.axis_size(spread_axis)
    length = shard.shape[0]
    padded = jnp.pad(shard, (0, (-length) % count))
    parts = lax.all_to_all(padded.reshape(count, -1), spread_axis, 0, 0, tiled=False)
    mine = butterfly_sum(jnp.sum(parts, axis=0), axes)
    spread = jnp.broadcast_to(mine[None], (count,) + mine.shape)
    whole = lax.all_to_all(spread, spread_axis, 0, 0, tiled=False)
    return whole.reshape(-1)[:length]


def butterfly_sum(shard, axes):
    for axis in axes:
        count = lax.axis_size(axis)
        step = 1
        while step < count:
            partners = [(i, i ^ step) for i in range(count)]
            shard = shard + lax.ppermute(shard, axis, partners)
            step *= 2
    return shard


def window_offsets():
    return [shift_by for shift_by in range(1, WINDOW + 1)] + [
        -shift_by for shift_by in range(1, WINDOW + 1)
    ]


def radial_tables(scaled):
    envelope = jnp.maximum(1.0 - scaled, 0.0)
    argument = 2.0 * jnp.minimum(scaled, 1.0) - 1.0
    first_kind = [jnp.ones_like(argument), argument]
    second_kind = [jnp.ones_like(argument), 2.0 * argument]
    for degree in range(2, RADIAL):
        first_kind.append(2.0 * argument * first_kind[-1] - first_kind[-2])
        second_kind.append(2.0 * argument * second_kind[-1] - second_kind[-2])
    values = []
    slopes = []
    for degree in range(RADIAL):
        damping = 1.0 / (1.0 + degree)
        values.append(envelope * envelope * first_kind[degree] * damping)
        derivative = -2.0 * envelope * first_kind[degree]
        if degree > 0:
            derivative = derivative + 2.0 * degree * envelope * envelope * second_kind[degree - 1]
        slopes.append(derivative * damping)
    return (jnp.stack(values, axis=1), jnp.stack(slopes, axis=1))


def shifted_stack(padded, atom_count):
    return jnp.stack(
        [padded[:, WINDOW + offset : WINDOW + offset + atom_count] for offset in window_offsets()]
    )


def pair_tables(padded, atom_count):
    offsets = window_offsets()
    here = padded[:, WINDOW : WINDOW + atom_count]
    there = shifted_stack(padded, atom_count)
    lift = jnp.array([0.0, 0.0, 1.0], jnp.float32)
    steps_z = jnp.array(offsets, jnp.float32) * spacing
    delta = there[:, :3, :] - here[None, :3, :] + steps_z[:, None, None] * lift[None, :, None]
    scaled = jnp.sum(delta * delta, axis=1) / cutoff_sq
    radial, slope = radial_tables(scaled)
    kinds = jnp.arange(SPECIES, dtype=jnp.float32)
    other = (there[:, 3:4, :] == kinds[None, :, None]).astype(jnp.float32)
    here_words = here[4].astype(jnp.int32)
    there_words = there[:, 4, :].astype(jnp.int32)
    upward = jnp.array([offset > 0 for offset in offsets])
    source = jnp.where(upward[:, None], here_words[None, :], there_words)
    bits = jnp.array([offset - 1 if offset > 0 else -offset - 1 for offset in offsets], jnp.int32)
    linked = jnp.bitwise_and(jnp.right_shift(source, bits[:, None]), 1).astype(jnp.float32)
    return (delta, radial, slope, other, linked)


def density(padded, atom_count):
    delta, radial, slope, other, linked = pair_tables(padded, atom_count)
    grid = jnp.sum(other[:, :, None, :] * (radial * linked[:, None, :])[:, None], axis=0)
    return grid.reshape(SPECIES * RADIAL, atom_count)


def slope_field(field_density, own_kinds, coefs):
    channels = field_density.shape[0]
    quad = coefs[:, :channels, :]
    both = quad + jnp.transpose(quad, (0, 2, 1))
    part = coefs[:, channels][:, :, None] + jnp.einsum(
        "zab,bn->zan", both, field_density, precision=HIGHEST
    ) / math.sqrt(channels)
    return jnp.sum(own_kinds[:, None, :] * part, axis=0)


def pull_force(slopes, slopes_pad, padded, own_kinds, atom_count):
    delta, radial, slope, other, linked = pair_tables(padded, atom_count)
    own_grid = slopes.reshape(SPECIES, RADIAL, atom_count)
    there_slopes = shifted_stack(slopes_pad, atom_count).reshape(
        2 * WINDOW, SPECIES, RADIAL, atom_count
    )
    outward = jnp.sum(other[:, :, None, :] * own_grid[None], axis=1)
    inward = jnp.sum(own_kinds[None, :, None, :] * there_slopes, axis=1)
    strength = jnp.sum((outward + inward) * slope, axis=1) * linked * (2.0 / cutoff_sq)
    return jnp.sum(strength[:, None, :] * delta, axis=0)


def back_terms(field_density, values, value_pad, padded, own_kinds, atom_count):
    delta, radial, slope, other, linked = pair_tables(padded, atom_count)
    there_values = shifted_stack(value_pad, atom_count)
    project = jnp.sum(delta * (values[None] - there_values), axis=1) * linked * (2.0 / cutoff_sq)
    channels = field_density.shape[0]
    weights = jnp.sum(
        other[:, :, None, :] * (slope * project[:, None, :])[:, None], axis=0
    ).reshape(channels, atom_count)
    masked = own_kinds[:, None, :] * field_density[None]
    cross = jnp.einsum("zbi,ai->zba", masked, weights, precision=HIGHEST)
    linear = jnp.sum(own_kinds[:, None, :] * weights[None], axis=2)
    both = (cross + jnp.transpose(cross, (0, 2, 1))) / math.sqrt(channels)
    return jnp.concatenate([both, linear[:, None, :]], axis=1)


def rotation(rho_bar, phi_bar, beta_norm, alpha_norm):
    rho_new = jnp.sqrt(rho_bar * rho_bar + beta_norm * beta_norm)
    cosine = rho_bar / rho_new
    sine_term = beta_norm / rho_new
    theta_term = sine_term * alpha_norm
    return (rho_new, theta_term, cosine * phi_bar, -cosine * alpha_norm, sine_term * phi_bar)


def shards(positions, species, atom_words, left_vector, right_vector, direction, solution, scalars):
    atom_count = positions.shape[2]
    coef_total = right_vector.size
    devices_all = lax.axis_size(SNAP) * lax.axis_size(BRICK)
    left_total = 3 * atom_count * positions.shape[0] * devices_all
    back_unit = force_unit * coef_total / left_total
    geometry = jnp.concatenate(
        [
            positions[0],
            species[0].astype(jnp.float32)[None],
            atom_words[0].astype(jnp.float32)[None],
        ],
        axis=0,
    )
    depth = 3 * WINDOW
    padded_all = with_halo(geometry, ((BRICK, 1),), depth)
    kind_values = jnp.arange(SPECIES, dtype=jnp.float32)
    ext_count = atom_count + 4 * WINDOW
    mid_count = atom_count + 2 * WINDOW
    density_ext = density(padded_all, ext_count)
    kinds_ext = (
        padded_all[3, WINDOW : WINDOW + ext_count][None, :] == kind_values[:, None]
    ).astype(jnp.float32)
    field_density = density_ext[:, 2 * WINDOW : 2 * WINDOW + atom_count]
    own_kinds = kinds_ext[:, 2 * WINDOW : 2 * WINDOW + atom_count]
    padded = padded_all[:, 2 * WINDOW : 4 * WINDOW + atom_count]
    mid_geometry = padded_all[:, WINDOW : 3 * WINDOW + mid_count]
    mid_kinds = kinds_ext[:, WINDOW : WINDOW + mid_count]
    left_ext = with_halo(left_vector[0], ((BRICK, 1),), WINDOW)
    alpha_norm = scalars[0]
    rho_bar = scalars[1]
    phi_bar = scalars[2]
    left_now = left_vector[0]
    right_now = right_vector
    direction_now = direction
    solution_now = solution
    for sweep in range(ITERS):
        slopes_ext = slope_field(density_ext, kinds_ext, right_now)
        force_ext = pull_force(
            slopes_ext[:, WINDOW : WINDOW + mid_count],
            slopes_ext,
            mid_geometry,
            mid_kinds,
            mid_count,
        )
        raw_pad = force_unit * force_ext - alpha_norm * left_ext
        raw_left = raw_pad[:, WINDOW : WINDOW + atom_count]
        local_terms = back_terms(field_density, raw_left, raw_pad, padded, own_kinds, atom_count)
        packed = jnp.concatenate(
            [local_terms.reshape(-1), jnp.sum(raw_left * raw_left)[None]]
        )
        packed = group_sum(packed, "brick_0", BUTTERFLY_ORDER)
        totals = packed[:-1].reshape(local_terms.shape)
        squares = packed[-1]
        beta_norm = jnp.sqrt(squares / left_total + tiny)
        left_now = raw_left / beta_norm
        right_raw = back_unit * totals / beta_norm - beta_norm * right_now
        left_ext = raw_pad / beta_norm
        alpha_norm = jnp.sqrt(jnp.sum(right_raw * right_raw) / coef_total + tiny)
        right_now = right_raw / alpha_norm
        rho_new, theta_term, phi_term, rho_bar, phi_bar = rotation(
            rho_bar, phi_bar, beta_norm, alpha_norm
        )
        solution_now = solution_now + phi_term / rho_new * direction_now
        direction_now = right_now - theta_term / rho_new * direction_now
    scalars_next = jnp.stack([alpha_norm, rho_bar, phi_bar])
    return (left_now[None], right_now, direction_now, solution_now, scalars_next)


def solution(mesh):
    torus = Mesh(
        mesh.devices.reshape(4, 2, 16, 2, 2), ("snap_0", "snap_1", "brick_0", "brick_1", "brick_2")
    )
    return jax.shard_map(
        shards,
        mesh=torus,
        in_specs=(
            P(SNAP, None, BRICK),
            P(SNAP, BRICK),
            P(SNAP, BRICK),
            P(SNAP, None, BRICK),
            P(),
            P(),
            P(),
            P(),
        ),
        out_specs=(P(SNAP, None, BRICK), P(), P(), P(), P()),
        check_vma=False,
    )
```

```python
import functools
import math

import jax
import jax.numpy as jnp
from jax import lax
from jax.sharding import Mesh
from jax.sharding import PartitionSpec as P

SPECIES = 5
RADIAL = 16
WINDOW = 15
ITERS = 3
SNAP = ("snap_0", "snap_1")
BRICK = ("brick_0", "brick_1", "brick_2")
SNAP_BRICK = ("snap_0", "snap_1", "brick_0", "brick_1", "brick_2")
BUTTERFLY_ORDER = ("brick_2", "snap_1", "brick_1")
SPREAD_AXES = ("snap_0", "brick_0")


cutoff_sq = 36.0
spacing = 0.25
force_unit = 0.015625
tiny = 1e-06
HIGHEST = lax.Precision.HIGHEST


def with_halo(cells, sides, width):
    for axis, dim in sides:
        count = lax.axis_size(axis)
        ends = count - 1
        head = lax.slice_in_dim(cells, 0, width, axis=dim)
        tail = lax.slice_in_dim(cells, cells.shape[dim] - width, cells.shape[dim], axis=dim)
        cells = jnp.concatenate(
            [
                lax.ppermute(tail, axis, [(i, (i + 1) % count) for i in range(ends)]),
                cells,
                lax.ppermute(head, axis, [((i + 1) % count, i) for i in range(ends)]),
            ],
            axis=dim,
        )
    return cells


def by_axis(shard, axes):
    return functools.reduce(lax.psum, axes, shard)


def group_sum(shard, spread_axis, axes):
    count = 1
    for axis in spread_axis:
        count *= lax.axis_size(axis)
    length = shard.shape[0]
    padded = jnp.pad(shard, (0, (-length) % count))
    parts = lax.all_to_all(padded.reshape(count, -1), spread_axis, 0, 0, tiled=False)
    mine = butterfly_sum(jnp.sum(parts, axis=0), axes)
    spread = jnp.broadcast_to(mine[None], (count,) + mine.shape)
    whole = lax.all_to_all(spread, spread_axis, 0, 0, tiled=False)
    return whole.reshape(-1)[:length]


def butterfly_sum(shard, axes):
    for axis in axes:
        count = lax.axis_size(axis)
        step = 1
        while step < count:
            partners = [(i, i ^ step) for i in range(count)]
            shard = shard + lax.ppermute(shard, axis, partners)
            step *= 2
    return shard


def window_offsets():
    return [shift_by for shift_by in range(1, WINDOW + 1)] + [
        -shift_by for shift_by in range(1, WINDOW + 1)
    ]


def radial_tables(scaled):
    envelope = jnp.maximum(1.0 - scaled, 0.0)
    argument = 2.0 * jnp.minimum(scaled, 1.0) - 1.0
    first_kind = [jnp.ones_like(argument), argument]
    second_kind = [jnp.ones_like(argument), 2.0 * argument]
    for degree in range(2, RADIAL):
        first_kind.append(2.0 * argument * first_kind[-1] - first_kind[-2])
        second_kind.append(2.0 * argument * second_kind[-1] - second_kind[-2])
    values = []
    slopes = []
    for degree in range(RADIAL):
        damping = 1.0 / (1.0 + degree)
        values.append(envelope * envelope * first_kind[degree] * damping)
        derivative = -2.0 * envelope * first_kind[degree]
        if degree > 0:
            derivative = derivative + 2.0 * degree * envelope * envelope * second_kind[degree - 1]
        slopes.append(derivative * damping)
    return (jnp.stack(values, axis=1), jnp.stack(slopes, axis=1))


def shifted_stack(padded, atom_count):
    return jnp.stack(
        [padded[:, WINDOW + offset : WINDOW + offset + atom_count] for offset in window_offsets()]
    )


def pair_tables(padded, atom_count):
    offsets = window_offsets()
    here = padded[:, WINDOW : WINDOW + atom_count]
    there = shifted_stack(padded, atom_count)
    lift = jnp.array([0.0, 0.0, 1.0], jnp.float32)
    steps_z = jnp.array(offsets, jnp.float32) * spacing
    delta = there[:, :3, :] - here[None, :3, :] + steps_z[:, None, None] * lift[None, :, None]
    scaled = jnp.sum(delta * delta, axis=1) / cutoff_sq
    radial, slope = radial_tables(scaled)
    kinds = jnp.arange(SPECIES, dtype=jnp.float32)
    other = (there[:, 3:4, :] == kinds[None, :, None]).astype(jnp.float32)
    here_words = here[4].astype(jnp.int32)
    there_words = there[:, 4, :].astype(jnp.int32)
    upward = jnp.array([offset > 0 for offset in offsets])
    source = jnp.where(upward[:, None], here_words[None, :], there_words)
    bits = jnp.array([offset - 1 if offset > 0 else -offset - 1 for offset in offsets], jnp.int32)
    linked = jnp.bitwise_and(jnp.right_shift(source, bits[:, None]), 1).astype(jnp.float32)
    return (delta, radial, slope, other, linked)


def density(padded, atom_count):
    delta, radial, slope, other, linked = pair_tables(padded, atom_count)
    grid = jnp.sum(other[:, :, None, :] * (radial * linked[:, None, :])[:, None], axis=0)
    return grid.reshape(SPECIES * RADIAL, atom_count)


def slope_field(field_density, own_kinds, coefs):
    channels = field_density.shape[0]
    quad = coefs[:, :channels, :]
    both = quad + jnp.transpose(quad, (0, 2, 1))
    part = coefs[:, channels][:, :, None] + jnp.einsum(
        "zab,bn->zan", both, field_density, precision=HIGHEST
    ) / math.sqrt(channels)
    return jnp.sum(own_kinds[:, None, :] * part, axis=0)


def pull_force(slopes, slopes_pad, padded, own_kinds, atom_count):
    delta, radial, slope, other, linked = pair_tables(padded, atom_count)
    own_grid = slopes.reshape(SPECIES, RADIAL, atom_count)
    outward = jnp.sum(other[:, :, None, :] * own_grid[None], axis=1)
    total = jnp.zeros((3, atom_count), jnp.float32)
    for index, offset in enumerate(window_offsets()):
        there = slopes_pad[:, WINDOW + offset : WINDOW + offset + atom_count].reshape(
            SPECIES, RADIAL, atom_count
        )
        inward = jnp.sum(own_kinds[:, None, :] * there, axis=0)
        strength = jnp.sum((outward[index] + inward) * slope[index], axis=0)
        strength = strength * linked[index] * (2.0 / cutoff_sq)
        total = total + strength[None, :] * delta[index]
    return total


def back_terms(field_density, values, value_pad, padded, own_kinds, atom_count):
    delta, radial, slope, other, linked = pair_tables(padded, atom_count)
    rows = [
        jnp.sum(delta[index] * (values - value_pad[:, WINDOW + offset : WINDOW + offset + atom_count]), axis=0)
        for index, offset in enumerate(window_offsets())
    ]
    project = jnp.stack(rows) * linked * (2.0 / cutoff_sq)
    channels = field_density.shape[0]
    weights = jnp.sum(
        other[:, :, None, :] * (slope * project[:, None, :])[:, None], axis=0
    ).reshape(channels, atom_count)
    masked = own_kinds[:, None, :] * field_density[None]
    cross = jnp.einsum("zbi,ai->zba", masked, weights, precision=HIGHEST)
    linear = jnp.sum(own_kinds[:, None, :] * weights[None], axis=2)
    both = (cross + jnp.transpose(cross, (0, 2, 1))) / math.sqrt(channels)
    return jnp.concatenate([both, linear[:, None, :]], axis=1)


def rotation(rho_bar, phi_bar, beta_norm, alpha_norm):
    rho_new = jnp.sqrt(rho_bar * rho_bar + beta_norm * beta_norm)
    cosine = rho_bar / rho_new
    sine_term = beta_norm / rho_new
    theta_term = sine_term * alpha_norm
    return (rho_new, theta_term, cosine * phi_bar, -cosine * alpha_norm, sine_term * phi_bar)


def shards(positions, species, atom_words, left_vector, right_vector, direction, solution, scalars):
    atom_count = positions.shape[2]
    coef_total = right_vector.size
    devices_all = lax.axis_size(SNAP) * lax.axis_size(BRICK)
    left_total = 3 * atom_count * positions.shape[0] * devices_all
    back_unit = force_unit * coef_total / left_total
    geometry = jnp.concatenate(
        [
            positions[0],
            species[0].astype(jnp.float32)[None],
            atom_words[0].astype(jnp.float32)[None],
        ],
        axis=0,
    )
    depth = 3 * WINDOW
    padded_all = with_halo(geometry, ((BRICK, 1),), depth)
    kind_values = jnp.arange(SPECIES, dtype=jnp.float32)
    ext_count = atom_count + 4 * WINDOW
    mid_count = atom_count + 2 * WINDOW
    density_ext = density(padded_all, ext_count)
    kinds_ext = (
        padded_all[3, WINDOW : WINDOW + ext_count][None, :] == kind_values[:, None]
    ).astype(jnp.float32)
    field_density = density_ext[:, 2 * WINDOW : 2 * WINDOW + atom_count]
    own_kinds = kinds_ext[:, 2 * WINDOW : 2 * WINDOW + atom_count]
    padded = padded_all[:, 2 * WINDOW : 4 * WINDOW + atom_count]
    mid_geometry = padded_all[:, WINDOW : 3 * WINDOW + mid_count]
    mid_kinds = kinds_ext[:, WINDOW : WINDOW + mid_count]
    left_ext = with_halo(left_vector[0], ((BRICK, 1),), WINDOW)
    alpha_norm = scalars[0]
    rho_bar = scalars[1]
    phi_bar = scalars[2]
    left_now = left_vector[0]
    right_now = right_vector
    direction_now = direction
    solution_now = solution
    for sweep in range(ITERS):
        slopes_ext = slope_field(density_ext, kinds_ext, right_now)
        force_ext = pull_force(
            slopes_ext[:, WINDOW : WINDOW + mid_count],
            slopes_ext,
            mid_geometry,
            mid_kinds,
            mid_count,
        )
        raw_pad = force_unit * force_ext - alpha_norm * left_ext
        raw_left = raw_pad[:, WINDOW : WINDOW + atom_count]
        local_terms = back_terms(field_density, raw_left, raw_pad, padded, own_kinds, atom_count)
        packed = jnp.concatenate(
            [local_terms.reshape(-1), jnp.sum(raw_left * raw_left)[None]]
        )
        packed = group_sum(packed, SPREAD_AXES, BUTTERFLY_ORDER)
        totals = packed[:-1].reshape(local_terms.shape)
        squares = packed[-1]
        beta_norm = jnp.sqrt(squares / left_total + tiny)
        left_now = raw_left / beta_norm
        right_raw = back_unit * totals / beta_norm - beta_norm * right_now
        left_ext = raw_pad / beta_norm
        alpha_norm = jnp.sqrt(jnp.sum(right_raw * right_raw) / coef_total + tiny)
        right_now = right_raw / alpha_norm
        rho_new, theta_term, phi_term, rho_bar, phi_bar = rotation(
            rho_bar, phi_bar, beta_norm, alpha_norm
        )
        solution_now = solution_now + phi_term / rho_new * direction_now
        direction_now = right_now - theta_term / rho_new * direction_now
    scalars_next = jnp.stack([alpha_norm, rho_bar, phi_bar])
    return (left_now[None], right_now, direction_now, solution_now, scalars_next)


def solution(mesh):
    torus = Mesh(
        mesh.devices.reshape(4, 2, 16, 2, 2), ("snap_0", "snap_1", "brick_0", "brick_1", "brick_2")
    )
    return jax.shard_map(
        shards,
        mesh=torus,
        in_specs=(
            P(SNAP, None, BRICK),
            P(SNAP, BRICK),
            P(SNAP, BRICK),
            P(SNAP, None, BRICK),
            P(),
            P(),
            P(),
            P(),
        ),
        out_specs=(P(SNAP, None, BRICK), P(), P(), P(), P()),
        check_vma=False,
    )
```

```python
import functools
import math

import jax
import jax.numpy as jnp
from jax import lax
from jax.sharding import Mesh
from jax.sharding import PartitionSpec as P

SPECIES = 5
RADIAL = 16
WINDOW = 15
ITERS = 3
SNAP = ("snap_0", "snap_1")
BRICK = ("brick_0", "brick_1", "brick_2")
SNAP_BRICK = ("snap_0", "snap_1", "brick_0", "brick_1", "brick_2")
BUTTERFLY_ORDER = ("brick_2", "snap_1", "brick_1")
SPREAD_AXES = ("snap_0", "brick_0")


cutoff_sq = 36.0
spacing = 0.25
force_unit = 0.015625
tiny = 1e-06
HIGHEST = lax.Precision.HIGHEST


def with_halo(cells, sides, width):
    for axis, dim in sides:
        count = lax.axis_size(axis)
        ends = count - 1
        head = lax.slice_in_dim(cells, 0, width, axis=dim)
        tail = lax.slice_in_dim(cells, cells.shape[dim] - width, cells.shape[dim], axis=dim)
        cells = jnp.concatenate(
            [
                lax.ppermute(tail, axis, [(i, (i + 1) % count) for i in range(ends)]),
                cells,
                lax.ppermute(head, axis, [((i + 1) % count, i) for i in range(ends)]),
            ],
            axis=dim,
        )
    return cells


def by_axis(shard, axes):
    return functools.reduce(lax.psum, axes, shard)


def group_sum(shard, spread_axis, axes):
    count = 1
    for axis in spread_axis:
        count *= lax.axis_size(axis)
    length = shard.shape[0]
    padded = jnp.pad(shard, (0, (-length) % count))
    parts = lax.all_to_all(padded.reshape(count, -1), spread_axis, 0, 0, tiled=False)
    mine = butterfly_sum(jnp.sum(parts, axis=0), axes)
    spread = jnp.broadcast_to(mine[None], (count,) + mine.shape)
    whole = lax.all_to_all(spread, spread_axis, 0, 0, tiled=False)
    return whole.reshape(-1)[:length]


def butterfly_sum(shard, axes):
    for axis in axes:
        count = lax.axis_size(axis)
        step = 1
        while step < count:
            partners = [(i, i ^ step) for i in range(count)]
            shard = shard + lax.ppermute(shard, axis, partners)
            step *= 2
    return shard


def window_offsets():
    return [shift_by for shift_by in range(1, WINDOW + 1)] + [
        -shift_by for shift_by in range(1, WINDOW + 1)
    ]


def radial_tables(scaled):
    envelope = jnp.maximum(1.0 - scaled, 0.0)
    argument = 2.0 * jnp.minimum(scaled, 1.0) - 1.0
    first_kind = [jnp.ones_like(argument), argument]
    second_kind = [jnp.ones_like(argument), 2.0 * argument]
    for degree in range(2, RADIAL):
        first_kind.append(2.0 * argument * first_kind[-1] - first_kind[-2])
        second_kind.append(2.0 * argument * second_kind[-1] - second_kind[-2])
    values = []
    slopes = []
    for degree in range(RADIAL):
        damping = 1.0 / (1.0 + degree)
        values.append(envelope * envelope * first_kind[degree] * damping)
        derivative = -2.0 * envelope * first_kind[degree]
        if degree > 0:
            derivative = derivative + 2.0 * degree * envelope * envelope * second_kind[degree - 1]
        slopes.append(derivative * damping)
    return (jnp.stack(values, axis=1), jnp.stack(slopes, axis=1))


def shifted_stack(padded, atom_count):
    return jnp.stack(
        [padded[:, WINDOW + offset : WINDOW + offset + atom_count] for offset in window_offsets()]
    )


def pair_tables(padded, atom_count):
    offsets = window_offsets()
    here = padded[:, WINDOW : WINDOW + atom_count]
    there = shifted_stack(padded, atom_count)
    lift = jnp.array([0.0, 0.0, 1.0], jnp.float32)
    steps_z = jnp.array(offsets, jnp.float32) * spacing
    delta = there[:, :3, :] - here[None, :3, :] + steps_z[:, None, None] * lift[None, :, None]
    scaled = jnp.sum(delta * delta, axis=1) / cutoff_sq
    radial, slope = radial_tables(scaled)
    kinds = jnp.arange(SPECIES, dtype=jnp.float32)
    other = (there[:, 3:4, :] == kinds[None, :, None]).astype(jnp.float32)
    here_words = here[4].astype(jnp.int32)
    there_words = there[:, 4, :].astype(jnp.int32)
    upward = jnp.array([offset > 0 for offset in offsets])
    source = jnp.where(upward[:, None], here_words[None, :], there_words)
    bits = jnp.array([offset - 1 if offset > 0 else -offset - 1 for offset in offsets], jnp.int32)
    linked = jnp.bitwise_and(jnp.right_shift(source, bits[:, None]), 1).astype(jnp.float32)
    return (delta, radial, slope, other, linked)


def density(padded, atom_count):
    delta, radial, slope, other, linked = pair_tables(padded, atom_count)
    grid = jnp.sum(other[:, :, None, :] * (radial * linked[:, None, :])[:, None], axis=0)
    return grid.reshape(SPECIES * RADIAL, atom_count)


def slope_field(field_density, own_kinds, coefs):
    channels = field_density.shape[0]
    quad = coefs[:, :channels, :]
    both = quad + jnp.transpose(quad, (0, 2, 1))
    part = coefs[:, channels][:, :, None] + jnp.einsum(
        "zab,bn->zan", both, field_density, precision=HIGHEST
    ) / math.sqrt(channels)
    return jnp.sum(own_kinds[:, None, :] * part, axis=0)


def cut_tables(tables, start, count):
    return tuple(lax.slice_in_dim(table, start, start + count, axis=table.ndim - 1) for table in tables)


def pull_force(slopes, slopes_pad, padded, own_kinds, atom_count, tables=None):
    if tables is None:
        tables = pair_tables(padded, atom_count)
    delta, radial, slope, other, linked = tables
    own_grid = slopes.reshape(SPECIES, RADIAL, atom_count)
    outward = jnp.sum(other[:, :, None, :] * own_grid[None], axis=1)
    total = jnp.zeros((3, atom_count), jnp.float32)
    for index, offset in enumerate(window_offsets()):
        there = slopes_pad[:, WINDOW + offset : WINDOW + offset + atom_count].reshape(
            SPECIES, RADIAL, atom_count
        )
        inward = jnp.sum(own_kinds[:, None, :] * there, axis=0)
        strength = jnp.sum((outward[index] + inward) * slope[index], axis=0)
        strength = strength * linked[index] * (2.0 / cutoff_sq)
        total = total + strength[None, :] * delta[index]
    return total


def back_terms(field_density, values, value_pad, padded, own_kinds, atom_count, tables=None):
    if tables is None:
        tables = pair_tables(padded, atom_count)
    delta, radial, slope, other, linked = tables
    channels = field_density.shape[0]
    weights = jnp.zeros((SPECIES, RADIAL, atom_count), jnp.float32)
    for index, offset in enumerate(window_offsets()):
        there = value_pad[:, WINDOW + offset : WINDOW + offset + atom_count]
        project = jnp.sum(delta[index] * (values - there), axis=0)
        project = project * linked[index] * (2.0 / cutoff_sq)
        weights = weights + other[index][:, None, :] * (slope[index] * project[None, :])[None]
    weights = weights.reshape(channels, atom_count)
    masked = own_kinds[:, None, :] * field_density[None]
    cross = jnp.einsum("zbi,ai->zba", masked, weights, precision=HIGHEST)
    linear = jnp.sum(own_kinds[:, None, :] * weights[None], axis=2)
    both = (cross + jnp.transpose(cross, (0, 2, 1))) / math.sqrt(channels)
    return jnp.concatenate([both, linear[:, None, :]], axis=1)


def rotation(rho_bar, phi_bar, beta_norm, alpha_norm):
    rho_new = jnp.sqrt(rho_bar * rho_bar + beta_norm * beta_norm)
    cosine = rho_bar / rho_new
    sine_term = beta_norm / rho_new
    theta_term = sine_term * alpha_norm
    return (rho_new, theta_term, cosine * phi_bar, -cosine * alpha_norm, sine_term * phi_bar)


def shards(positions, species, atom_words, left_vector, right_vector, direction, solution, scalars):
    atom_count = positions.shape[2]
    coef_total = right_vector.size
    devices_all = lax.axis_size(SNAP) * lax.axis_size(BRICK)
    left_total = 3 * atom_count * positions.shape[0] * devices_all
    back_unit = force_unit * coef_total / left_total
    geometry = jnp.concatenate(
        [
            positions[0],
            species[0].astype(jnp.float32)[None],
            atom_words[0].astype(jnp.float32)[None],
        ],
        axis=0,
    )
    depth = 3 * WINDOW
    padded_all = with_halo(geometry, ((BRICK, 1),), depth)
    kind_values = jnp.arange(SPECIES, dtype=jnp.float32)
    ext_count = atom_count + 4 * WINDOW
    mid_count = atom_count + 2 * WINDOW
    tables_ext = pair_tables(padded_all, ext_count)
    _, radial_ext, _, other_ext, linked_ext = tables_ext
    density_ext = jnp.sum(
        other_ext[:, :, None, :] * (radial_ext * linked_ext[:, None, :])[:, None], axis=0
    ).reshape(SPECIES * RADIAL, ext_count)
    tables_mid = cut_tables(tables_ext, WINDOW, mid_count)
    tables_own = cut_tables(tables_ext, 2 * WINDOW, atom_count)
    kinds_ext = (
        padded_all[3, WINDOW : WINDOW + ext_count][None, :] == kind_values[:, None]
    ).astype(jnp.float32)
    field_density = density_ext[:, 2 * WINDOW : 2 * WINDOW + atom_count]
    own_kinds = kinds_ext[:, 2 * WINDOW : 2 * WINDOW + atom_count]
    padded = padded_all[:, 2 * WINDOW : 4 * WINDOW + atom_count]
    mid_geometry = padded_all[:, WINDOW : 3 * WINDOW + mid_count]
    mid_kinds = kinds_ext[:, WINDOW : WINDOW + mid_count]
    left_ext = with_halo(left_vector[0], ((BRICK, 1),), WINDOW)
    alpha_norm = scalars[0]
    rho_bar = scalars[1]
    phi_bar = scalars[2]
    left_now = left_vector[0]
    right_now = right_vector
    direction_now = direction
    solution_now = solution
    for sweep in range(ITERS):
        slopes_ext = slope_field(density_ext, kinds_ext, right_now)
        force_ext = pull_force(
            slopes_ext[:, WINDOW : WINDOW + mid_count],
            slopes_ext,
            mid_geometry,
            mid_kinds,
            mid_count,
            tables_mid,
        )
        raw_pad = force_unit * force_ext - alpha_norm * left_ext
        raw_left = raw_pad[:, WINDOW : WINDOW + atom_count]
        local_terms = back_terms(
            field_density, raw_left, raw_pad, padded, own_kinds, atom_count, tables_own
        )
        packed = jnp.concatenate(
            [local_terms.reshape(-1), jnp.sum(raw_left * raw_left)[None]]
        )
        packed = group_sum(packed, SPREAD_AXES, BUTTERFLY_ORDER)
        totals = packed[:-1].reshape(local_terms.shape)
        squares = packed[-1]
        beta_norm = jnp.sqrt(squares / left_total + tiny)
        left_now = raw_left / beta_norm
        right_raw = back_unit * totals / beta_norm - beta_norm * right_now
        left_ext = raw_pad / beta_norm
        alpha_norm = jnp.sqrt(jnp.sum(right_raw * right_raw) / coef_total + tiny)
        right_now = right_raw / alpha_norm
        rho_new, theta_term, phi_term, rho_bar, phi_bar = rotation(
            rho_bar, phi_bar, beta_norm, alpha_norm
        )
        solution_now = solution_now + phi_term / rho_new * direction_now
        direction_now = right_now - theta_term / rho_new * direction_now
    scalars_next = jnp.stack([alpha_norm, rho_bar, phi_bar])
    return (left_now[None], right_now, direction_now, solution_now, scalars_next)


def solution(mesh):
    torus = Mesh(
        mesh.devices.reshape(4, 2, 16, 2, 2), ("snap_0", "snap_1", "brick_0", "brick_1", "brick_2")
    )
    return jax.shard_map(
        shards,
        mesh=torus,
        in_specs=(
            P(SNAP, None, BRICK),
            P(SNAP, BRICK),
            P(SNAP, BRICK),
            P(SNAP, None, BRICK),
            P(),
            P(),
            P(),
            P(),
        ),
        out_specs=(P(SNAP, None, BRICK), P(), P(), P(), P()),
        check_vma=False,
    )
```

```python
import functools
import math

import jax
import jax.numpy as jnp
from jax import lax
from jax.sharding import Mesh
from jax.sharding import PartitionSpec as P

SPECIES = 5
RADIAL = 16
WINDOW = 15
ITERS = 3
SNAP = ("snap_0", "snap_1")
BRICK = ("brick_0", "brick_1", "brick_2")
SNAP_BRICK = ("snap_0", "snap_1", "brick_0", "brick_1", "brick_2")
BUTTERFLY_ORDER = ("brick_2", "snap_1", "brick_1")
SPREAD_AXES = ("snap_0", "brick_0")


cutoff_sq = 36.0
spacing = 0.25
force_unit = 0.015625
tiny = 1e-06
HIGHEST = lax.Precision.HIGHEST


def with_halo(cells, sides, width):
    for axis, dim in sides:
        count = lax.axis_size(axis)
        ends = count - 1
        head = lax.slice_in_dim(cells, 0, width, axis=dim)
        tail = lax.slice_in_dim(cells, cells.shape[dim] - width, cells.shape[dim], axis=dim)
        cells = jnp.concatenate(
            [
                lax.ppermute(tail, axis, [(i, (i + 1) % count) for i in range(ends)]),
                cells,
                lax.ppermute(head, axis, [((i + 1) % count, i) for i in range(ends)]),
            ],
            axis=dim,
        )
    return cells


def by_axis(shard, axes):
    return functools.reduce(lax.psum, axes, shard)


def group_sum(shard, spread_axis, axes):
    count = 1
    for axis in spread_axis:
        count *= lax.axis_size(axis)
    length = shard.shape[0]
    padded = jnp.pad(shard, (0, (-length) % count))
    parts = lax.all_to_all(padded.reshape(count, -1), spread_axis, 0, 0, tiled=False)
    mine = butterfly_sum(jnp.sum(parts, axis=0), axes)
    spread = jnp.broadcast_to(mine[None], (count,) + mine.shape)
    whole = lax.all_to_all(spread, spread_axis, 0, 0, tiled=False)
    return whole.reshape(-1)[:length]


def butterfly_sum(shard, axes):
    for axis in axes:
        count = lax.axis_size(axis)
        step = 1
        while step < count:
            partners = [(i, i ^ step) for i in range(count)]
            shard = shard + lax.ppermute(shard, axis, partners)
            step *= 2
    return shard


def window_offsets():
    return [shift_by for shift_by in range(1, WINDOW + 1)] + [
        -shift_by for shift_by in range(1, WINDOW + 1)
    ]


def radial_tables(scaled):
    envelope = jnp.maximum(1.0 - scaled, 0.0)
    argument = 2.0 * jnp.minimum(scaled, 1.0) - 1.0
    first_kind = [jnp.ones_like(argument), argument]
    second_kind = [jnp.ones_like(argument), 2.0 * argument]
    for degree in range(2, RADIAL):
        first_kind.append(2.0 * argument * first_kind[-1] - first_kind[-2])
        second_kind.append(2.0 * argument * second_kind[-1] - second_kind[-2])
    values = []
    slopes = []
    for degree in range(RADIAL):
        damping = 1.0 / (1.0 + degree)
        values.append(envelope * envelope * first_kind[degree] * damping)
        derivative = -2.0 * envelope * first_kind[degree]
        if degree > 0:
            derivative = derivative + 2.0 * degree * envelope * envelope * second_kind[degree - 1]
        slopes.append(derivative * damping)
    return (jnp.stack(values, axis=1), jnp.stack(slopes, axis=1))


def shifted_stack(padded, atom_count):
    return jnp.stack(
        [padded[:, WINDOW + offset : WINDOW + offset + atom_count] for offset in window_offsets()]
    )


def pair_tables(padded, atom_count):
    offsets = window_offsets()
    here = padded[:, WINDOW : WINDOW + atom_count]
    there = shifted_stack(padded, atom_count)
    lift = jnp.array([0.0, 0.0, 1.0], jnp.float32)
    steps_z = jnp.array(offsets, jnp.float32) * spacing
    delta = there[:, :3, :] - here[None, :3, :] + steps_z[:, None, None] * lift[None, :, None]
    scaled = jnp.sum(delta * delta, axis=1) / cutoff_sq
    radial, slope = radial_tables(scaled)
    kinds = jnp.arange(SPECIES, dtype=jnp.float32)
    other = (there[:, 3:4, :] == kinds[None, :, None]).astype(jnp.float32)
    here_words = here[4].astype(jnp.int32)
    there_words = there[:, 4, :].astype(jnp.int32)
    upward = jnp.array([offset > 0 for offset in offsets])
    source = jnp.where(upward[:, None], here_words[None, :], there_words)
    bits = jnp.array([offset - 1 if offset > 0 else -offset - 1 for offset in offsets], jnp.int32)
    linked = jnp.bitwise_and(jnp.right_shift(source, bits[:, None]), 1).astype(jnp.float32)
    return (delta, radial, slope, other, linked)


def density(padded, atom_count):
    delta, radial, slope, other, linked = pair_tables(padded, atom_count)
    grid = jnp.sum(other[:, :, None, :] * (radial * linked[:, None, :])[:, None], axis=0)
    return grid.reshape(SPECIES * RADIAL, atom_count)


def slope_field(field_density, own_kinds, coefs):
    channels = field_density.shape[0]
    quad = coefs[:, :channels, :]
    both = quad + jnp.transpose(quad, (0, 2, 1))
    part = coefs[:, channels][:, :, None] + jnp.einsum(
        "zab,bn->zan", both, field_density, precision=HIGHEST
    ) / math.sqrt(channels)
    return jnp.sum(own_kinds[:, None, :] * part, axis=0)


def cut_tables(tables, start, count):
    return tuple(lax.slice_in_dim(table, start, start + count, axis=table.ndim - 1) for table in tables)


def pull_force(slopes, slopes_pad, padded, own_kinds, atom_count, tables=None):
    if tables is None:
        tables = pair_tables(padded, atom_count)
    delta, radial, slope, other, linked = tables
    own_grid = slopes.reshape(SPECIES, RADIAL, atom_count)
    outward = jnp.sum(other[:, :, None, :] * own_grid[None], axis=1)
    total = jnp.zeros((3, atom_count), jnp.float32)
    for index, offset in enumerate(window_offsets()):
        there = slopes_pad[:, WINDOW + offset : WINDOW + offset + atom_count].reshape(
            SPECIES, RADIAL, atom_count
        )
        inward = jnp.sum(own_kinds[:, None, :] * there, axis=0)
        strength = jnp.sum((outward[index] + inward) * slope[index], axis=0)
        strength = strength * linked[index] * (2.0 / cutoff_sq)
        total = total + strength[None, :] * delta[index]
    return total


def back_terms(field_density, values, value_pad, padded, own_kinds, atom_count, tables=None):
    if tables is None:
        tables = pair_tables(padded, atom_count)
    delta, radial, slope, other, linked = tables
    channels = field_density.shape[0]
    weights = jnp.zeros((SPECIES, RADIAL, atom_count), jnp.float32)
    for index, offset in enumerate(window_offsets()):
        there = value_pad[:, WINDOW + offset : WINDOW + offset + atom_count]
        project = jnp.sum(delta[index] * (values - there), axis=0)
        project = project * linked[index] * (2.0 / cutoff_sq)
        weights = weights + other[index][:, None, :] * (slope[index] * project[None, :])[None]
    weights = weights.reshape(channels, atom_count)
    masked = own_kinds[:, None, :] * field_density[None]
    cross = jnp.einsum("zbi,ai->zba", masked, weights, precision=HIGHEST)
    linear = jnp.sum(own_kinds[:, None, :] * weights[None], axis=2)
    both = (cross + jnp.transpose(cross, (0, 2, 1))) / math.sqrt(channels)
    return jnp.concatenate([both, linear[:, None, :]], axis=1)


def rotation(rho_bar, phi_bar, beta_norm, alpha_norm):
    rho_new = jnp.sqrt(rho_bar * rho_bar + beta_norm * beta_norm)
    cosine = rho_bar / rho_new
    sine_term = beta_norm / rho_new
    theta_term = sine_term * alpha_norm
    return (rho_new, theta_term, cosine * phi_bar, -cosine * alpha_norm, sine_term * phi_bar)


def shards(positions, species, atom_words, left_vector, right_vector, direction, solution, scalars):
    atom_count = positions.shape[2]
    coef_total = right_vector.size
    devices_all = lax.axis_size(SNAP) * lax.axis_size(BRICK)
    left_total = 3 * atom_count * positions.shape[0] * devices_all
    back_unit = force_unit * coef_total / left_total
    geometry = jnp.concatenate(
        [
            positions[0],
            species[0].astype(jnp.float32)[None],
            atom_words[0].astype(jnp.float32)[None],
        ],
        axis=0,
    )
    depth = 3 * WINDOW
    stacked_all = with_halo(jnp.concatenate([geometry, left_vector[0]], axis=0), ((BRICK, 1),), depth)
    padded_all = stacked_all[:5]
    kind_values = jnp.arange(SPECIES, dtype=jnp.float32)
    ext_count = atom_count + 4 * WINDOW
    mid_count = atom_count + 2 * WINDOW
    tables_ext = pair_tables(padded_all, ext_count)
    _, radial_ext, _, other_ext, linked_ext = tables_ext
    density_ext = jnp.sum(
        other_ext[:, :, None, :] * (radial_ext * linked_ext[:, None, :])[:, None], axis=0
    ).reshape(SPECIES * RADIAL, ext_count)
    tables_mid = cut_tables(tables_ext, WINDOW, mid_count)
    tables_own = cut_tables(tables_ext, 2 * WINDOW, atom_count)
    kinds_ext = (
        padded_all[3, WINDOW : WINDOW + ext_count][None, :] == kind_values[:, None]
    ).astype(jnp.float32)
    field_density = density_ext[:, 2 * WINDOW : 2 * WINDOW + atom_count]
    own_kinds = kinds_ext[:, 2 * WINDOW : 2 * WINDOW + atom_count]
    padded = padded_all[:, 2 * WINDOW : 4 * WINDOW + atom_count]
    mid_geometry = padded_all[:, WINDOW : 3 * WINDOW + mid_count]
    mid_kinds = kinds_ext[:, WINDOW : WINDOW + mid_count]
    left_ext = stacked_all[5:, 2 * WINDOW : 4 * WINDOW + atom_count]
    alpha_norm = scalars[0]
    rho_bar = scalars[1]
    phi_bar = scalars[2]
    left_now = left_vector[0]
    right_now = right_vector
    direction_now = direction
    solution_now = solution
    for sweep in range(ITERS):
        slopes_ext = slope_field(density_ext, kinds_ext, right_now)
        force_ext = pull_force(
            slopes_ext[:, WINDOW : WINDOW + mid_count],
            slopes_ext,
            mid_geometry,
            mid_kinds,
            mid_count,
            tables_mid,
        )
        raw_pad = force_unit * force_ext - alpha_norm * left_ext
        raw_left = raw_pad[:, WINDOW : WINDOW + atom_count]
        local_terms = back_terms(
            field_density, raw_left, raw_pad, padded, own_kinds, atom_count, tables_own
        )
        packed = jnp.concatenate(
            [local_terms.reshape(-1), jnp.sum(raw_left * raw_left)[None]]
        )
        packed = group_sum(packed, SPREAD_AXES, BUTTERFLY_ORDER)
        totals = packed[:-1].reshape(local_terms.shape)
        squares = packed[-1]
        beta_norm = jnp.sqrt(squares / left_total + tiny)
        left_now = raw_left / beta_norm
        right_raw = back_unit * totals / beta_norm - beta_norm * right_now
        left_ext = raw_pad / beta_norm
        alpha_norm = jnp.sqrt(jnp.sum(right_raw * right_raw) / coef_total + tiny)
        right_now = right_raw / alpha_norm
        rho_new, theta_term, phi_term, rho_bar, phi_bar = rotation(
            rho_bar, phi_bar, beta_norm, alpha_norm
        )
        solution_now = solution_now + phi_term / rho_new * direction_now
        direction_now = right_now - theta_term / rho_new * direction_now
    scalars_next = jnp.stack([alpha_norm, rho_bar, phi_bar])
    return (left_now[None], right_now, direction_now, solution_now, scalars_next)


def solution(mesh):
    torus = Mesh(
        mesh.devices.reshape(4, 2, 16, 2, 2), ("snap_0", "snap_1", "brick_0", "brick_1", "brick_2")
    )
    return jax.shard_map(
        shards,
        mesh=torus,
        in_specs=(
            P(SNAP, None, BRICK),
            P(SNAP, BRICK),
            P(SNAP, BRICK),
            P(SNAP, None, BRICK),
            P(),
            P(),
            P(),
            P(),
        ),
        out_specs=(P(SNAP, None, BRICK), P(), P(), P(), P()),
        check_vma=False,
    )
```
